256 devices in a mesh: row: 16 (over y, x_lo, core), col: 16 (over x_hi, z).
Axes of the slice: x: 4 (x_hi: 2, x_lo: 2; x = x_hi * 2 + x_lo), y: 4, z: 8, core: 2. Of those that a mesh axis runs over, the one named last changes fastest.
Arguments:
- stored_blocks: float32 [512, 16, 128, 128], P('row', 'col'), may hold values from -1.8 to 1.8
- block_cols: int32 [512, 16], P('row', 'col'), may hold values from 0 to 31, as said below
- storage_map: int32 [512, 16], P('row', 'col'), may hold values from 0 to 1, as said below
Outputs:
- square_part: float32 [512, 16, 128, 128], P('row', 'col')
The draws below stay inside these ranges and needn't reach their ends.
Inputs may be any that keep to these rules, and one draw needn't show every extreme that they name: The block pattern is symmetric: block (R, q) with column C = q * 32 + block_cols[R, q] has block_cols[C, R // 32] == R mod 32; every slab pairs its block rows with its block columns one to one; block_cols[R, R // 32] == R mod 32. Of a block and its mirror image exactly one has storage_map 1; blocks on the diagonal have 1.
All inputs are finite; a program needn't handle non-finite values.
Results may differ from the reference program's by a relative error of at most 0.0001.
Values sent between devices are 32-bit elements; how exact they have to be, the bound alone decides.
No kernel may reach another device: no remote copies, remote signals or barrier semaphores. Data moves between devices by JAX's collectives and lax.ppermute only.
A program may use at most 128 MiB of HBM per device.

```python
import jax
import jax.numpy as jnp
from jax import lax

BS = 128
BLK = 32
STEPS = 4
SLABS = 16
NBLK = 512


def build_pattern(key):
    base_key = jax.random.fold_in(key, 7)
    perm_key, shift_key, swap_key, coin_key = jax.random.split(base_key, 4)
    sigma = jax.vmap(lambda k: jax.random.permutation(k, BLK))(jax.random.split(perm_key, SLABS)).astype(jnp.int32)
    inverse = jnp.argsort(sigma, axis=1).astype(jnp.int32)
    offsets = jax.random.randint(shift_key, (SLABS,), 0, BLK).astype(jnp.int32)
    offset_gap = offsets[:, None] - offsets[None, :]
    moved_count = 2 * max(1, BLK // 8)
    slot_ids = jnp.arange(BLK, dtype=jnp.int32)
    partner = jnp.where(slot_ids < moved_count, jnp.bitwise_xor(slot_ids, 1), slot_ids).astype(jnp.int32)

    def make_swap(pair_index):
        shuffled = jax.random.permutation(jax.random.fold_in(swap_key, pair_index), BLK).astype(jnp.int32)
        return jnp.zeros((BLK,), jnp.int32).at[shuffled].set(shuffled[partner])
    slab_ids = jnp.arange(SLABS, dtype=jnp.int32)
    lower_slab = jnp.minimum(slab_ids[:, None], slab_ids[None, :])
    upper_slab = jnp.maximum(slab_ids[:, None], slab_ids[None, :])
    swaps = jax.vmap(make_swap)((lower_slab * SLABS + upper_slab).reshape(-1)).reshape(SLABS, SLABS, BLK)
    diagonal_pair = slab_ids[:, None] == slab_ids[None, :]
    swaps = jnp.where(diagonal_pair[:, :, None], slot_ids[None, None, :], swaps).astype(jnp.int32)
    total_rows = BLK * SLABS
    row_ids = jnp.arange(total_rows, dtype=jnp.int32)
    slab_of = row_ids // BLK
    local_row = row_ids % BLK
    placed = sigma[slab_of, local_row]
    row_gap = offset_gap[slab_of, :]
    pair_swaps = swaps[slab_of]
    start_slot = jnp.broadcast_to(placed[:, None, None], (total_rows, SLABS, 1))
    forward = jnp.take_along_axis(pair_swaps, start_slot, axis=2)[:, :, 0] - row_gap
    back_slot = ((placed[:, None] - row_gap) % BLK)[:, :, None]
    backward = jnp.take_along_axis(pair_swaps, back_slot, axis=2)[:, :, 0]
    upward = slab_of[:, None] < slab_ids[None, :]
    target = jnp.where(upward, forward, backward) % BLK
    cols = inverse[slab_ids[None, :], target].astype(jnp.int32)
    column_global = slab_ids[None, :] * BLK + cols
    row_global = jnp.broadcast_to(row_ids[:, None], cols.shape)
    first_index = jnp.minimum(row_global, column_global)
    second_index = jnp.maximum(row_global, column_global)
    pair_key = (first_index * total_rows + second_index).reshape(-1)
    coins = jax.vmap(lambda p: jax.random.randint(jax.random.fold_in(coin_key, p), (), 0, 2))(pair_key)
    coins = coins.reshape(cols.shape).astype(jnp.int32)
    stored = jnp.where(row_global < column_global, coins, jnp.where(row_global > column_global, 1 - coins, 1))
    return (cols, stored.astype(jnp.int32))


def draw_block_cols(key, part):
    cols, stored = build_pattern(key)
    return cols


def draw_storage_map(key, part):
    cols, stored = build_pattern(key)
    return stored


def block_scale(stream_key, extent, shards, smallest, high):
    level, own = 1.0, jax.random.fold_in(stream_key, 6)
    for position, blocks in shards:
        steps = jnp.exp(jax.random.uniform(jax.random.fold_in(own, position), (blocks,), jnp.float32, smallest / len(shards), high / len(shards)))
        level = level * jnp.repeat(steps, extent[position] // blocks).reshape([-1 if axis == position else 1 for axis in range(len(extent))])
    return level


def noise(own_key, dims, deviation, limit, cuts=(), held_as=jnp.bfloat16):
    factor_of = block_scale(own_key, dims, cuts, -0.22, 0.18) if cuts else 1.0
    result = jax.random.normal(own_key, dims, jnp.float32) * deviation * factor_of
    return jnp.minimum(jnp.maximum(result, -limit), limit).astype(held_as)


def setup_inputs(seed: int = 0) -> dict:
    seeds = jax.random.split(jax.random.key(seed), 4)
    return {
        "stored_blocks": noise(seeds[0], (NBLK, SLABS, BS, BS), 0.3, 1.8, ((0, 16), (1, 16)), jnp.float32),
        "block_cols": draw_block_cols(jax.random.fold_in(seeds[3], 71), 0),
        "storage_map": draw_storage_map(jax.random.fold_in(seeds[3], 71), 0),
    }


def reference(stored_blocks, block_cols, storage_map):
    held = stored_blocks * storage_map.astype(jnp.float32)[:, :, None, None]
    total_rows = held.shape[0]
    row_ids = jnp.arange(total_rows, dtype=jnp.int32)
    slab_ids = jnp.arange(SLABS, dtype=jnp.int32)
    mirror_rows = slab_ids[None, :] * BLK + block_cols
    mirror_slabs = jnp.broadcast_to((row_ids // BLK)[:, None], block_cols.shape)
    mirrored = held[mirror_rows, mirror_slabs]
    density = held + jnp.swapaxes(mirrored, 2, 3)
    total = jnp.zeros(held.shape, jnp.float32)
    for step in range(STEPS):
        kappa = ((row_ids // BLK + step) % SLABS).astype(jnp.int32)
        left = density[row_ids, kappa]
        inner = (kappa * BLK + block_cols[row_ids, kappa]).astype(jnp.int32)
        right = density[inner]
        match = block_cols[inner] == block_cols
        term = jnp.einsum('rik,rqkj->rqij', left, right, precision=lax.Precision.HIGHEST)
        total = total + jnp.where(match[:, :, None, None], term, jnp.float32(0.0))
    return total
```

```python
import jax
import jax.numpy as jnp
from jax import lax
from jax.sharding import PartitionSpec as P

STEPS = 4


def shifted(block, axis, distance):
    size = lax.axis_size(axis)
    route = [((i + distance) % size, i) for i in range(size)]
    return lax.ppermute(block, axis, route)


def transposed(block, rows, cols):
    route = [(b * cols + a, a * cols + b) for a in range(rows) for b in range(cols)]
    return lax.ppermute(block, ("row", "col"), route)


def gathered_cols(block_cols, rows, cols):
    local_rows = block_cols.shape[0]
    flat = lax.all_gather(block_cols[:, 0], ("row", "col"), axis=0, tiled=True)
    grid = flat.reshape(rows, cols, local_rows)
    return jnp.transpose(grid, (0, 2, 1)).reshape(rows * local_rows, cols)


def shards(stored_blocks, block_cols, storage_map):
    rows = lax.axis_size("row")
    cols = lax.axis_size("col")
    local_rows = stored_blocks.shape[0]
    bs = stored_blocks.shape[-1]
    row_index = lax.axis_index("row")
    col_index = lax.axis_index("col")

    all_cols = gathered_cols(block_cols, rows, cols)

    held = stored_blocks[:, 0] * storage_map.astype(jnp.float32)[:, :, None]
    arrived = transposed(held, rows, cols)
    mirrored = arrived[block_cols[:, 0]]
    density = held + jnp.swapaxes(mirrored, 1, 2)

    chunk = local_rows // cols
    pieces = density.reshape(cols, chunk, bs, bs)
    spread = lax.all_to_all(pieces, "col", 0, 0, tiled=True)
    window = (row_index + jnp.arange(STEPS, dtype=jnp.int32)) % cols
    mine = spread[window]
    left_all = lax.all_gather(mine, "col", axis=0, tiled=False)
    left_all = jnp.transpose(left_all, (1, 0, 2, 3, 4)).reshape(STEPS, local_rows, bs, bs)

    rights = [density] + [shifted(density, "row", step) for step in range(1, STEPS)]

    own_cols = block_cols[:, 0]
    total = jnp.zeros(density.shape, jnp.float32)
    for step in range(STEPS):
        kappa = (row_index + step) % cols
        inner = lax.dynamic_index_in_dim(all_cols, kappa, 1, keepdims=False)
        inner = lax.dynamic_slice_in_dim(inner, row_index * local_rows, local_rows)
        right = rights[step][inner]
        panel_cols = lax.dynamic_index_in_dim(all_cols, col_index, 1, keepdims=False)
        panel_cols = lax.dynamic_slice_in_dim(panel_cols, kappa * local_rows, local_rows)
        match = panel_cols[inner] == own_cols
        term = jnp.einsum("rik,rkj->rij", left_all[step], right, precision=lax.Precision.HIGHEST)
        total = total + jnp.where(match[:, None, None], term, jnp.float32(0.0))
    return total[:, None]


def solution(mesh):
    return jax.shard_map(
        shards,
        mesh=mesh,
        in_specs=(P("row", "col", None, None), P("row", "col"), P("row", "col")),
        out_specs=P("row", "col", None, None),
        check_vma=False,
    )
```

```python
import jax
import jax.numpy as jnp
from jax import lax
from jax.sharding import PartitionSpec as P

STEPS = 4


def shifted(block, axis, distance):
    size = lax.axis_size(axis)
    route = [((i + distance) % size, i) for i in range(size)]
    return lax.ppermute(block, axis, route)


def transposed(block, rows, cols):
    route = [(b * cols + a, a * cols + b) for a in range(rows) for b in range(cols)]
    return lax.ppermute(block, ("row", "col"), route)


def shards(stored_blocks, block_cols, storage_map):
    rows = lax.axis_size("row")
    cols = lax.axis_size("col")
    local_rows = stored_blocks.shape[0]
    bs = stored_blocks.shape[-1]
    row_index = lax.axis_index("row")

    row_cols = lax.all_gather(block_cols, "col", axis=1, tiled=True)
    col_cols = lax.all_gather(block_cols, "row", axis=0, tiled=True)[:, 0]

    held = stored_blocks[:, 0] * storage_map.astype(jnp.float32)[:, :, None]
    arrived = transposed(held, rows, cols)
    mirrored = arrived[block_cols[:, 0]]
    density = held + jnp.swapaxes(mirrored, 1, 2)

    chunk = local_rows // cols
    pieces = density.reshape(cols, chunk, bs, bs)
    spread = lax.all_to_all(pieces, "col", 0, 0, tiled=True)
    window = (row_index + jnp.arange(STEPS, dtype=jnp.int32)) % cols
    mine = spread[window]
    left_all = lax.all_gather(mine, "col", axis=0, tiled=False)
    left_all = jnp.transpose(left_all, (1, 0, 2, 3, 4)).reshape(STEPS, local_rows, bs, bs)

    one = shifted(density, "row", 1)
    two = shifted(density, "row", 2)
    three = shifted(two, "row", 1)
    rights = [density, one, two, three]

    own_cols = block_cols[:, 0]
    total = jnp.zeros(density.shape, jnp.float32)
    for step in range(STEPS):
        kappa = (row_index + step) % cols
        inner = lax.dynamic_index_in_dim(row_cols, kappa, 1, keepdims=False)
        right = rights[step][inner]
        panel_cols = lax.dynamic_slice_in_dim(col_cols, kappa * local_rows, local_rows)
        match = panel_cols[inner] == own_cols
        term = jnp.einsum("rik,rkj->rij", left_all[step], right, precision=lax.Precision.HIGHEST)
        total = total + jnp.where(match[:, None, None], term, jnp.float32(0.0))
    return total[:, None]


def solution(mesh):
    return jax.shard_map(
        shards,
        mesh=mesh,
        in_specs=(P("row", "col", None, None), P("row", "col"), P("row", "col")),
        out_specs=P("row", "col", None, None),
        check_vma=False,
    )
```

```python
import jax
import jax.numpy as jnp
from jax import lax
from jax.sharding import PartitionSpec as P

STEPS = 4


def shifted(block, axis, distance):
    size = lax.axis_size(axis)
    route = [((i + distance) % size, i) for i in range(size)]
    return lax.ppermute(block, axis, route)


def transposed(block, rows, cols, window):
    route = [
        (b * cols + a, a * cols + b)
        for a in range(rows)
        for b in range(cols)
        if ((b - a) % cols < STEPS) == window
    ]
    return lax.ppermute(block, ("row", "col"), route)


def shards(stored_blocks, block_cols, storage_map):
    rows = lax.axis_size("row")
    cols = lax.axis_size("col")
    local_rows = stored_blocks.shape[0]
    bs = stored_blocks.shape[-1]
    row_index = lax.axis_index("row")
    col_index = lax.axis_index("col")

    row_cols = lax.all_gather(block_cols, "col", axis=1, tiled=True)
    col_cols = lax.all_gather(block_cols, "row", axis=0, tiled=True)[:, 0]

    held = stored_blocks[:, 0] * storage_map.astype(jnp.float32)[:, :, None]
    part = transposed(held, rows, cols, True)
    rest = transposed(held, rows, cols, False)
    sources = held + jnp.swapaxes(part[block_cols[:, 0]], 1, 2)
    density = held + jnp.swapaxes((part + rest)[block_cols[:, 0]], 1, 2)

    chunk = local_rows // cols
    pieces = sources.reshape(cols, chunk, bs, bs)
    received = []
    for distance in range(cols):
        piece = lax.dynamic_index_in_dim(pieces, (col_index + distance) % cols, 0, keepdims=False)
        if distance == 0:
            received.append(piece)
            continue
        route = [
            (a * cols + (a + s) % cols, a * cols + (a + s + distance) % cols)
            for a in range(rows)
            for s in range(STEPS)
        ]
        received.append(lax.ppermute(piece, ("row", "col"), route))
    received = jnp.stack(received)
    window = (col_index - row_index - jnp.arange(STEPS, dtype=jnp.int32)) % cols
    mine = received[window]
    left_all = lax.all_gather(mine, "col", axis=0, tiled=False)
    left_all = jnp.transpose(left_all, (1, 0, 2, 3, 4)).reshape(STEPS, local_rows, bs, bs)

    one = shifted(density, "row", 1)
    two = shifted(density, "row", 2)
    three = shifted(two, "row", 1)
    rights = [density, one, two, three]

    own_cols = block_cols[:, 0]
    total = jnp.zeros(density.shape, jnp.float32)
    for step in range(STEPS):
        kappa = (row_index + step) % cols
        inner = lax.dynamic_index_in_dim(row_cols, kappa, 1, keepdims=False)
        right = rights[step][inner]
        panel_cols = lax.dynamic_slice_in_dim(col_cols, kappa * local_rows, local_rows)
        match = panel_cols[inner] == own_cols
        term = jnp.einsum("rik,rkj->rij", left_all[step], right, precision=lax.Precision.HIGHEST)
        total = total + jnp.where(match[:, None, None], term, jnp.float32(0.0))
    return total[:, None]


def solution(mesh):
    return jax.shard_map(
        shards,
        mesh=mesh,
        in_specs=(P("row", "col", None, None), P("row", "col"), P("row", "col")),
        out_specs=P("row", "col", None, None),
        check_vma=False,
    )
```

```python
import jax
import jax.numpy as jnp
from jax import lax
from jax.sharding import PartitionSpec as P

STEPS = 4


def shifted(block, axis, distance):
    size = lax.axis_size(axis)
    route = [((i + distance) % size, i) for i in range(size)]
    return lax.ppermute(block, axis, route)


def transposed(block, rows, cols):
    route = [(b * cols + a, a * cols + b) for a in range(rows) for b in range(cols)]
    return lax.ppermute(block, ("row", "col"), route)


def shards(stored_blocks, block_cols, storage_map):
    rows = lax.axis_size("row")
    cols = lax.axis_size("col")
    local_rows = stored_blocks.shape[0]
    bs = stored_blocks.shape[-1]
    row_index = lax.axis_index("row")
    col_index = lax.axis_index("col")

    row_cols = lax.all_gather(block_cols, "col", axis=1, tiled=True)
    col_cols = lax.all_gather(block_cols, "row", axis=0, tiled=True)[:, 0]

    held = stored_blocks[:, 0] * storage_map.astype(jnp.float32)[:, :, None]
    arrived = transposed(held, rows, cols)
    density = held + jnp.swapaxes(arrived[block_cols[:, 0]], 1, 2)

    inverse = jnp.zeros((local_rows,), jnp.int32).at[block_cols[:, 0]].set(
        jnp.arange(local_rows, dtype=jnp.int32)
    )
    mirror_out = jnp.swapaxes(held[inverse], 1, 2)
    chunk = local_rows // cols
    pieces = jnp.stack([held, mirror_out]).reshape(2, cols, chunk, bs, bs)
    spread = lax.all_to_all(pieces, "col", 1, 1, tiled=True)
    mine = []
    for step in range(STEPS):
        own = lax.dynamic_index_in_dim(spread[0], (row_index + step) % cols, 0, keepdims=False)
        far = lax.dynamic_index_in_dim(spread[1], (row_index - step) % cols, 0, keepdims=False)
        if step:
            far = shifted(far, "row", step)
        mine.append(own + far)
    mine = jnp.stack(mine)
    left_all = lax.all_gather(mine, "col", axis=0, tiled=False)
    left_all = jnp.transpose(left_all, (1, 0, 2, 3, 4)).reshape(STEPS, local_rows, bs, bs)

    one = shifted(density, "row", 1)
    two = shifted(density, "row", 2)
    three = shifted(two, "row", 1)
    rights = [density, one, two, three]

    own_cols = block_cols[:, 0]
    total = jnp.zeros(density.shape, jnp.float32)
    for step in range(STEPS):
        kappa = (row_index + step) % cols
        inner = lax.dynamic_index_in_dim(row_cols, kappa, 1, keepdims=False)
        right = rights[step][inner]
        panel_cols = lax.dynamic_slice_in_dim(col_cols, kappa * local_rows, local_rows)
        match = panel_cols[inner] == own_cols
        term = jnp.einsum("rik,rkj->rij", left_all[step], right, precision=lax.Precision.HIGHEST)
        total = total + jnp.where(match[:, None, None], term, jnp.float32(0.0))
    return total[:, None]


def solution(mesh):
    return jax.shard_map(
        shards,
        mesh=mesh,
        in_specs=(P("row", "col", None, None), P("row", "col"), P("row", "col")),
        out_specs=P("row", "col", None, None),
        check_vma=False,
    )
```

```python
import jax
import jax.numpy as jnp
from jax import lax
from jax.sharding import PartitionSpec as P

STEPS = 4


def shifted(block, axis, distance):
    size = lax.axis_size(axis)
    route = [((i + distance) % size, i) for i in range(size)]
    return lax.ppermute(block, axis, route)


def transposed(block, rows, cols):
    route = [(b * cols + a, a * cols + b) for a in range(rows) for b in range(cols)]
    return lax.ppermute(block, ("row", "col"), route)


def shards(stored_blocks, block_cols, storage_map):
    rows = lax.axis_size("row")
    cols = lax.axis_size("col")
    local_rows = stored_blocks.shape[0]
    bs = stored_blocks.shape[-1]
    row_index = lax.axis_index("row")
    col_index = lax.axis_index("col")

    row_cols = lax.all_gather(block_cols, "col", axis=1, tiled=True)
    col_cols = lax.all_gather(block_cols, "row", axis=0, tiled=True)[:, 0]

    held = stored_blocks[:, 0] * storage_map.astype(jnp.float32)[:, :, None]
    inverse = jnp.zeros((local_rows,), jnp.int32).at[block_cols[:, 0]].set(
        jnp.arange(local_rows, dtype=jnp.int32)
    )
    mirror_out = jnp.swapaxes(held[inverse], 1, 2)
    chunk = local_rows // cols
    pieces = jnp.stack([held, mirror_out]).reshape(2, cols, chunk, bs, bs)
    spread = lax.all_to_all(pieces, "col", 1, 1, tiled=True)
    first = jnp.swapaxes(spread[0], 0, 1)
    second = lax.all_to_all(first, "row", 1, 1, tiled=True)
    arrived = lax.all_to_all(second, "col", 1, 0, tiled=True).reshape(local_rows, bs, bs)
    density = held + jnp.swapaxes(arrived[block_cols[:, 0]], 1, 2)
    mine = []
    for step in range(STEPS):
        own = lax.dynamic_index_in_dim(spread[0], (row_index + step) % cols, 0, keepdims=False)
        far = lax.dynamic_index_in_dim(spread[1], (row_index - step) % cols, 0, keepdims=False)
        if step:
            far = shifted(far, "row", step)
        mine.append(own + far)
    mine = jnp.stack(mine)
    left_all = lax.all_gather(mine, "col", axis=0, tiled=False)
    left_all = jnp.transpose(left_all, (1, 0, 2, 3, 4)).reshape(STEPS, local_rows, bs, bs)

    one = shifted(density, "row", 1)
    two = shifted(density, "row", 2)
    three = shifted(two, "row", 1)
    rights = [density, one, two, three]

    own_cols = block_cols[:, 0]
    total = jnp.zeros(density.shape, jnp.float32)
    for step in range(STEPS):
        kappa = (row_index + step) % cols
        inner = lax.dynamic_index_in_dim(row_cols, kappa, 1, keepdims=False)
        right = rights[step][inner]
        panel_cols = lax.dynamic_slice_in_dim(col_cols, kappa * local_rows, local_rows)
        match = panel_cols[inner] == own_cols
        term = jnp.einsum("rik,rkj->rij", left_all[step], right, precision=lax.Precision.HIGHEST)
        total = total + jnp.where(match[:, None, None], term, jnp.float32(0.0))
    return total[:, None]


def solution(mesh):
    return jax.shard_map(
        shards,
        mesh=mesh,
        in_specs=(P("row", "col", None, None), P("row", "col"), P("row", "col")),
        out_specs=P("row", "col", None, None),
        check_vma=False,
    )
```

```python
import jax
import jax.numpy as jnp
from jax import lax
from jax.sharding import PartitionSpec as P

STEPS = 4
EXTRA = 8


def shifted(block, axis, distance):
    size = lax.axis_size(axis)
    route = [((i + distance) % size, i) for i in range(size)]
    return lax.ppermute(block, axis, route)


def transposed(block, rows, cols):
    route = [(b * cols + a, a * cols + b) for a in range(rows) for b in range(cols)]
    return lax.ppermute(block, ("row", "col"), route)


def shards(stored_blocks, block_cols, storage_map):
    rows = lax.axis_size("row")
    cols = lax.axis_size("col")
    local_rows = stored_blocks.shape[0]
    bs = stored_blocks.shape[-1]
    row_index = lax.axis_index("row")

    held = stored_blocks[:, 0] * storage_map.astype(jnp.float32)[:, :, None]
    own_cols = block_cols[:, 0]
    tag = jnp.zeros((local_rows, EXTRA, bs), jnp.float32).at[:, 0, 0].set(own_cols.astype(jnp.float32))
    blank = jnp.zeros((local_rows, EXTRA, bs), jnp.float32)
    inverse = jnp.zeros((local_rows,), jnp.int32).at[block_cols[:, 0]].set(
        jnp.arange(local_rows, dtype=jnp.int32)
    )
    mirror_out = jnp.swapaxes(held[inverse], 1, 2)
    chunk = local_rows // cols
    pieces = jnp.stack([
        jnp.concatenate([held, tag], axis=1),
        jnp.concatenate([mirror_out, blank], axis=1),
    ]).reshape(2, cols, chunk, bs + EXTRA, bs)
    spread = lax.all_to_all(pieces, "col", 1, 1, tiled=True)
    first = jnp.swapaxes(spread[0, :, :, :bs], 0, 1)
    second = lax.all_to_all(first, "row", 1, 1, tiled=True)
    arrived = lax.all_to_all(second, "col", 1, 0, tiled=True).reshape(local_rows, bs, bs)
    density = held + jnp.swapaxes(arrived[block_cols[:, 0]], 1, 2)
    mine = []
    for step in range(STEPS):
        own = lax.dynamic_index_in_dim(spread[0], (row_index + step) % cols, 0, keepdims=False)
        far = lax.dynamic_index_in_dim(spread[1], (row_index - step) % cols, 0, keepdims=False)
        if step:
            far = shifted(far, "row", step)
        mine.append(own + far)
    mine = jnp.stack(mine)
    left_all = lax.all_gather(mine, "col", axis=0, tiled=False)
    left_all = jnp.transpose(left_all, (1, 0, 2, 3, 4)).reshape(STEPS, local_rows, bs + EXTRA, bs)
    density = jnp.concatenate([density, tag], axis=1)

    one = shifted(density, "row", 1)
    two = shifted(density, "row", 2)
    three = shifted(two, "row", 1)
    rights = [density, one, two, three]

    total = jnp.zeros((local_rows, bs, bs), jnp.float32)
    for step in range(STEPS):
        left = left_all[step]
        inner = left[:, bs, 0].astype(jnp.int32)
        right = rights[step][inner]
        match = right[:, bs, 0].astype(jnp.int32) == own_cols
        term = jnp.einsum(
            "rik,rkj->rij", left[:, :bs], right[:, :bs], precision=lax.Precision.HIGHEST
        )
        total = total + jnp.where(match[:, None, None], term, jnp.float32(0.0))
    return total[:, None]


def solution(mesh):
    return jax.shard_map(
        shards,
        mesh=mesh,
        in_specs=(P("row", "col", None, None), P("row", "col"), P("row", "col")),
        out_specs=P("row", "col", None, None),
        check_vma=False,
    )
```

```python
import jax
import jax.numpy as jnp
from jax import lax
from jax.sharding import PartitionSpec as P

STEPS = 4
EXTRA = 8


def shifted(block, axis, distance):
    size = lax.axis_size(axis)
    route = [((i + distance) % size, i) for i in range(size)]
    return lax.ppermute(block, axis, route)


def transposed(block, rows, cols):
    route = [(b * cols + a, a * cols + b) for a in range(rows) for b in range(cols)]
    return lax.ppermute(block, ("row", "col"), route)


def shards(stored_blocks, block_cols, storage_map):
    rows = lax.axis_size("row")
    cols = lax.axis_size("col")
    local_rows = stored_blocks.shape[0]
    bs = stored_blocks.shape[-1]
    row_index = lax.axis_index("row")

    held = stored_blocks[:, 0] * storage_map.astype(jnp.float32)[:, :, None]
    own_cols = block_cols[:, 0]
    tag = jnp.zeros((local_rows, EXTRA, bs), jnp.float32).at[:, 0, 0].set(own_cols.astype(jnp.float32))
    blank = jnp.zeros((local_rows, EXTRA, bs), jnp.float32)
    inverse = jnp.zeros((local_rows,), jnp.int32).at[block_cols[:, 0]].set(
        jnp.arange(local_rows, dtype=jnp.int32)
    )
    mirror_out = jnp.swapaxes(held[inverse], 1, 2)
    chunk = local_rows // cols
    pieces = jnp.stack([
        jnp.concatenate([held, tag], axis=1),
        jnp.concatenate([mirror_out, blank], axis=1),
    ]).reshape(2, cols, chunk, bs + EXTRA, bs)
    spread = lax.all_to_all(pieces, "col", 1, 1, tiled=True)
    first = jnp.swapaxes(spread[0, :, :, :bs], 0, 1)
    second = lax.all_to_all(first, "row", 1, 1, tiled=True)
    arrived = lax.all_to_all(second, "col", 1, 0, tiled=True).reshape(local_rows, bs, bs)
    density = held + jnp.swapaxes(arrived[block_cols[:, 0]], 1, 2)
    mine = []
    for step in range(STEPS):
        own = lax.dynamic_index_in_dim(spread[0], (row_index + step) % cols, 0, keepdims=False)
        far = lax.dynamic_index_in_dim(spread[1], (row_index - step) % cols, 0, keepdims=False)
        if step:
            far = shifted(far, "row", step)
        mine.append(own + far)
    mine = jnp.stack(mine)
    left_all = lax.all_gather(mine, "col", axis=0, tiled=False)
    left_all = jnp.transpose(left_all, (1, 0, 2, 3, 4)).reshape(STEPS, local_rows, bs + EXTRA, bs)
    density = jnp.concatenate([density, tag], axis=1)

    two = shifted(density, "row", 2)
    odd_three = lax.ppermute(density, "row", [((i + 3) % rows, i) for i in range(1, rows, 2)])
    to_even = lax.ppermute(jnp.stack([density, two]), "row", [(i + 1, i) for i in range(0, rows, 2)])
    to_odd = lax.ppermute(two, "row", [(i, i + 1) for i in range(0, rows, 2)])
    even = row_index % 2 == 0
    one = jnp.where(even, to_even[0], to_odd)
    three = jnp.where(even, to_even[1], odd_three)
    rights = [density, one, two, three]

    total = jnp.zeros((local_rows, bs, bs), jnp.float32)
    for step in range(STEPS):
        left = left_all[step]
        inner = left[:, bs, 0].astype(jnp.int32)
        right = rights[step][inner]
        match = right[:, bs, 0].astype(jnp.int32) == own_cols
        term = jnp.einsum(
            "rik,rkj->rij", left[:, :bs], right[:, :bs], precision=lax.Precision.HIGHEST
        )
        total = total + jnp.where(match[:, None, None], term, jnp.float32(0.0))
    return total[:, None]


def solution(mesh):
    return jax.shard_map(
        shards,
        mesh=mesh,
        in_specs=(P("row", "col", None, None), P("row", "col"), P("row", "col")),
        out_specs=P("row", "col", None, None),
        check_vma=False,
    )
```

```python
import jax
import jax.numpy as jnp
from jax import lax
from jax.sharding import PartitionSpec as P

STEPS = 4
EXTRA = 8


def shifted(block, axis, distance):
    size = lax.axis_size(axis)
    route = [((i + distance) % size, i) for i in range(size)]
    return lax.ppermute(block, axis, route)


def transposed(block, rows, cols):
    route = [(b * cols + a, a * cols + b) for a in range(rows) for b in range(cols)]
    return lax.ppermute(block, ("row", "col"), route)


def shards(stored_blocks, block_cols, storage_map):
    rows = lax.axis_size("row")
    cols = lax.axis_size("col")
    local_rows = stored_blocks.shape[0]
    bs = stored_blocks.shape[-1]
    row_index = lax.axis_index("row")

    held = stored_blocks[:, 0] * storage_map.astype(jnp.float32)[:, :, None]
    own_cols = block_cols[:, 0]
    tag = jnp.zeros((local_rows, EXTRA, bs), jnp.float32).at[:, 0, 0].set(own_cols.astype(jnp.float32))
    blank = jnp.zeros((local_rows, EXTRA, bs), jnp.float32)
    inverse = jnp.zeros((local_rows,), jnp.int32).at[block_cols[:, 0]].set(
        jnp.arange(local_rows, dtype=jnp.int32)
    )
    mirror_out = jnp.swapaxes(held[inverse], 1, 2)
    chunk = local_rows // cols
    pieces = jnp.stack([
        jnp.concatenate([held, tag], axis=1),
        jnp.concatenate([mirror_out, blank], axis=1),
    ]).reshape(2, cols, chunk, bs + EXTRA, bs)
    spread = lax.all_to_all(pieces, "col", 1, 1, tiled=True)
    first = jnp.swapaxes(spread[0, :, :, :bs], 0, 1)
    second = lax.all_to_all(first, "row", 1, 1, tiled=True)
    arrived = lax.all_to_all(second, "col", 1, 0, tiled=True).reshape(local_rows, bs, bs)
    density = held + jnp.swapaxes(arrived[block_cols[:, 0]], 1, 2)
    mine = []
    for step in range(STEPS):
        own = lax.dynamic_index_in_dim(spread[0], (row_index + step) % cols, 0, keepdims=False)
        far = lax.dynamic_index_in_dim(spread[1], (row_index - step) % cols, 0, keepdims=False)
        if step:
            far = shifted(far, "row", step)
        mine.append(own + far)
    mine = jnp.stack(mine)
    left_all = lax.all_gather(mine, "col", axis=0, tiled=False)
    left_all = jnp.transpose(left_all, (1, 0, 2, 3, 4)).reshape(STEPS, local_rows, bs + EXTRA, bs)
    density = jnp.concatenate([density, tag], axis=1)

    one = shifted(density, "row", 1)
    two = shifted(density, "row", 2)
    three = shifted(density, "row", 3)
    rights = [density, one, two, three]

    total = jnp.zeros((local_rows, bs, bs), jnp.float32)
    for step in range(STEPS):
        left = left_all[step]
        inner = left[:, bs, 0].astype(jnp.int32)
        right = rights[step][inner]
        match = right[:, bs, 0].astype(jnp.int32) == own_cols
        term = jnp.einsum(
            "rik,rkj->rij", left[:, :bs], right[:, :bs], precision=lax.Precision.HIGHEST
        )
        total = total + jnp.where(match[:, None, None], term, jnp.float32(0.0))
    return total[:, None]


def solution(mesh):
    return jax.shard_map(
        shards,
        mesh=mesh,
        in_specs=(P("row", "col", None, None), P("row", "col"), P("row", "col")),
        out_specs=P("row", "col", None, None),
        check_vma=False,
    )
```

```python
import jax
import jax.numpy as jnp
from jax import lax
from jax.sharding import PartitionSpec as P

STEPS = 4
EXTRA = 8


def shifted(block, axis, distance):
    size = lax.axis_size(axis)
    route = [((i + distance) % size, i) for i in range(size)]
    return lax.ppermute(block, axis, route)


def transposed(block, rows, cols):
    route = [(b * cols + a, a * cols + b) for a in range(rows) for b in range(cols)]
    return lax.ppermute(block, ("row", "col"), route)


def shards(stored_blocks, block_cols, storage_map):
    rows = lax.axis_size("row")
    cols = lax.axis_size("col")
    local_rows = stored_blocks.shape[0]
    bs = stored_blocks.shape[-1]
    row_index = lax.axis_index("row")

    held = stored_blocks[:, 0] * storage_map.astype(jnp.float32)[:, :, None]
    own_cols = block_cols[:, 0]
    tag = jnp.zeros((local_rows, EXTRA, bs), jnp.float32).at[:, 0, 0].set(own_cols.astype(jnp.float32))
    blank = jnp.zeros((local_rows, EXTRA, bs), jnp.float32)
    inverse = jnp.zeros((local_rows,), jnp.int32).at[block_cols[:, 0]].set(
        jnp.arange(local_rows, dtype=jnp.int32)
    )
    mirror_out = held[inverse]
    chunk = local_rows // cols
    pieces = jnp.stack([
        jnp.concatenate([held, tag], axis=1),
        jnp.concatenate([mirror_out, blank], axis=1),
    ]).reshape(2, cols, chunk, bs + EXTRA, bs)
    spread = lax.all_to_all(pieces, "col", 1, 1, tiled=True)
    first = jnp.swapaxes(spread[0, :, :, :bs], 0, 1)
    second = lax.all_to_all(first, "row", 1, 1, tiled=True)
    arrived = lax.all_to_all(second, "col", 1, 0, tiled=True).reshape(local_rows, bs, bs)
    density = held + jnp.swapaxes(arrived[block_cols[:, 0]], 1, 2)
    mine = []
    for step in range(STEPS):
        own = lax.dynamic_index_in_dim(spread[0], (row_index + step) % cols, 0, keepdims=False)
        far = lax.dynamic_index_in_dim(spread[1], (row_index - step) % cols, 0, keepdims=False)
        far = jnp.concatenate([jnp.swapaxes(far[:, :bs], 1, 2), far[:, bs:]], axis=1)
        if step:
            far = shifted(far, "row", step)
        mine.append(own + far)
    mine = jnp.stack(mine)
    left_all = lax.all_gather(mine, "col", axis=0, tiled=False)
    left_all = jnp.transpose(left_all, (1, 0, 2, 3, 4)).reshape(STEPS, local_rows, bs + EXTRA, bs)
    density = jnp.concatenate([density, tag], axis=1)

    one = shifted(density, "row", 1)
    two = shifted(density, "row", 2)
    three = shifted(two, "row", 1)
    rights = [density, one, two, three]

    total = jnp.zeros((local_rows, bs, bs), jnp.float32)
    for step in range(STEPS):
        left = left_all[step]
        inner = left[:, bs, 0].astype(jnp.int32)
        right = rights[step][inner]
        match = right[:, bs, 0].astype(jnp.int32) == own_cols
        term = jnp.einsum(
            "rik,rkj->rij", left[:, :bs], right[:, :bs], precision=lax.Precision.HIGHEST
        )
        total = total + jnp.where(match[:, None, None], term, jnp.float32(0.0))
    return total[:, None]


def solution(mesh):
    return jax.shard_map(
        shards,
        mesh=mesh,
        in_specs=(P("row", "col", None, None), P("row", "col"), P("row", "col")),
        out_specs=P("row", "col", None, None),
        check_vma=False,
    )
```

```python
import jax
import jax.numpy as jnp
from jax import lax
from jax.sharding import PartitionSpec as P

STEPS = 4
EXTRA = 8


def shifted(block, axis, distance):
    size = lax.axis_size(axis)
    route = [((i + distance) % size, i) for i in range(size)]
    return lax.ppermute(block, axis, route)


def transposed(block, rows, cols):
    route = [(b * cols + a, a * cols + b) for a in range(rows) for b in range(cols)]
    return lax.ppermute(block, ("row", "col"), route)


def shards(stored_blocks, block_cols, storage_map):
    rows = lax.axis_size("row")
    cols = lax.axis_size("col")
    local_rows = stored_blocks.shape[0]
    bs = stored_blocks.shape[-1]
    row_index = lax.axis_index("row")

    held = stored_blocks[:, 0] * storage_map.astype(jnp.float32)[:, :, None]
    own_cols = block_cols[:, 0]
    inverse = jnp.zeros((local_rows,), jnp.int32).at[own_cols].set(jnp.arange(local_rows, dtype=jnp.int32))
    mirror_out = jnp.swapaxes(held[inverse], 1, 2)
    chunk = local_rows // cols
    span = chunk * bs
    tags = jnp.zeros((cols, EXTRA, bs), jnp.float32).at[:, 0, :chunk].set(
        own_cols.astype(jnp.float32).reshape(cols, chunk)
    )
    pieces = jnp.concatenate([
        held.reshape(cols, span, bs),
        mirror_out.reshape(cols, span, bs),
        tags,
    ], axis=1)
    spread = lax.all_to_all(pieces, "col", 0, 0, tiled=True)
    first = jnp.swapaxes(spread[:, :span].reshape(cols, chunk, bs, bs), 0, 1)
    second = lax.all_to_all(first, "row", 1, 1, tiled=True)
    arrived = lax.all_to_all(second, "col", 1, 0, tiled=True).reshape(local_rows, bs, bs)
    density = held + jnp.swapaxes(arrived[own_cols], 1, 2)
    mine = []
    for step in range(STEPS):
        own = lax.dynamic_index_in_dim(spread, (row_index + step) % cols, 0, keepdims=False)
        far = lax.dynamic_index_in_dim(spread, (row_index - step) % cols, 0, keepdims=False)[span:2 * span]
        if step:
            far = shifted(far, "row", step)
        blocks = (own[:span] + far).reshape(chunk, bs, bs)
        marks = jnp.zeros((chunk, EXTRA, bs), jnp.float32).at[:, 0, 0].set(own[2 * span, :chunk])
        mine.append(jnp.concatenate([blocks, marks], axis=1))
    mine = jnp.stack(mine)
    left_all = lax.all_gather(mine, "col", axis=0, tiled=False)
    left_all = jnp.transpose(left_all, (1, 0, 2, 3, 4)).reshape(STEPS, local_rows, bs + EXTRA, bs)

    one = shifted(density, "row", 1)
    two = shifted(density, "row", 2)
    three = shifted(two, "row", 1)
    rights = [density, one, two, three]
    cols_two = shifted(own_cols, "row", 2)
    right_cols = [own_cols, shifted(own_cols, "row", 1), cols_two, shifted(cols_two, "row", 1)]

    total = jnp.zeros((local_rows, bs, bs), jnp.float32)
    for step in range(STEPS):
        left = left_all[step]
        inner = left[:, bs, 0].astype(jnp.int32)
        right = rights[step][inner]
        match = right_cols[step][inner] == own_cols
        term = jnp.einsum("rik,rkj->rij", left[:, :bs], right, precision=lax.Precision.HIGHEST)
        total = total + jnp.where(match[:, None, None], term, jnp.float32(0.0))
    return total[:, None]


def solution(mesh):
    return jax.shard_map(
        shards,
        mesh=mesh,
        in_specs=(P("row", "col", None, None), P("row", "col"), P("row", "col")),
        out_specs=P("row", "col", None, None),
        check_vma=False,
    )
```

```python
import jax
import jax.numpy as jnp
from jax import lax
from jax.sharding import PartitionSpec as P

STEPS = 4
EXTRA = 8


def shifted(block, axis, distance):
    size = lax.axis_size(axis)
    route = [((i + distance) % size, i) for i in range(size)]
    return lax.ppermute(block, axis, route)


def transposed(block, rows, cols):
    route = [(b * cols + a, a * cols + b) for a in range(rows) for b in range(cols)]
    return lax.ppermute(block, ("row", "col"), route)


def shards(stored_blocks, block_cols, storage_map):
    rows = lax.axis_size("row")
    cols = lax.axis_size("col")
    local_rows = stored_blocks.shape[0]
    bs = stored_blocks.shape[-1]
    row_index = lax.axis_index("row")

    held = stored_blocks[:, 0] * storage_map.astype(jnp.float32)[:, :, None]
    own_cols = block_cols[:, 0]
    inverse = jnp.zeros((local_rows,), jnp.int32).at[own_cols].set(jnp.arange(local_rows, dtype=jnp.int32))
    mirror_out = jnp.swapaxes(held[inverse], 1, 2)
    chunk = local_rows // cols
    span = chunk * bs
    tags = jnp.zeros((cols, EXTRA, bs), jnp.float32).at[:, 0, :chunk].set(
        own_cols.astype(jnp.float32).reshape(cols, chunk)
    )
    pieces = jnp.concatenate([
        held.reshape(cols, span, bs),
        mirror_out.reshape(cols, span, bs),
        tags,
    ], axis=1)
    spread = lax.all_to_all(pieces, "col", 0, 0, tiled=True)
    first = jnp.swapaxes(spread[:, :span].reshape(cols, chunk, bs, bs), 0, 1)
    second = lax.all_to_all(first, "row", 1, 1, tiled=True)
    arrived = lax.all_to_all(second, "col", 1, 0, tiled=True).reshape(local_rows, bs, bs)
    density = held + jnp.swapaxes(arrived[own_cols], 1, 2)
    mine = []
    for step in range(STEPS):
        own = lax.dynamic_index_in_dim(spread, (row_index + step) % cols, 0, keepdims=False)
        far = lax.dynamic_index_in_dim(spread, (row_index - step) % cols, 0, keepdims=False)[span:2 * span]
        if step:
            far = shifted(far, "row", step)
        blocks = (own[:span] + far).reshape(chunk, bs, bs)
        marks = jnp.zeros((chunk, EXTRA, bs), jnp.float32).at[:, 0, 0].set(own[2 * span, :chunk])
        mine.append(jnp.concatenate([blocks, marks], axis=1))
    mine = jnp.stack(mine)
    left_all = lax.all_gather(mine, "col", axis=0, tiled=False)
    left_all = jnp.transpose(left_all, (1, 0, 2, 3, 4)).reshape(STEPS, local_rows, bs + EXTRA, bs)

    one = shifted(density, "row", 1)
    two = shifted(density, "row", 2)
    three = shifted(two, "row", 1)
    rights = [density, one, two, three]
    cols_two = shifted(own_cols, "row", 2)
    right_cols = [own_cols, shifted(own_cols, "row", 1), cols_two, shifted(cols_two, "row", 1)]

    total = jnp.zeros((local_rows, bs, bs), jnp.float32)
    for step in range(STEPS):
        left = left_all[step]
        inner = left[:, bs, 0].astype(jnp.int32)
        right = rights[step][inner]
        match = right_cols[step][inner] == own_cols
        term = jnp.einsum("rik,rkj->rij", left[:, :bs], right, precision=lax.Precision.HIGH)
        total = total + jnp.where(match[:, None, None], term, jnp.float32(0.0))
    return total[:, None]


def solution(mesh):
    return jax.shard_map(
        shards,
        mesh=mesh,
        in_specs=(P("row", "col", None, None), P("row", "col"), P("row", "col")),
        out_specs=P("row", "col", None, None),
        check_vma=False,
    )
```

```python
import jax
import jax.numpy as jnp
from jax import lax
from jax.sharding import PartitionSpec as P

STEPS = 4
EXTRA = 8


def shifted(block, axis, distance):
    size = lax.axis_size(axis)
    route = [((i + distance) % size, i) for i in range(size)]
    return lax.ppermute(block, axis, route)


def transposed(block, rows, cols):
    route = [(b * cols + a, a * cols + b) for a in range(rows) for b in range(cols)]
    return lax.ppermute(block, ("row", "col"), route)


def shards(stored_blocks, block_cols, storage_map):
    rows = lax.axis_size("row")
    cols = lax.axis_size("col")
    local_rows = stored_blocks.shape[0]
    bs = stored_blocks.shape[-1]
    row_index = lax.axis_index("row")

    held = stored_blocks[:, 0] * storage_map.astype(jnp.float32)[:, :, None]
    own_cols = block_cols[:, 0]
    inverse = jnp.zeros((local_rows,), jnp.int32).at[own_cols].set(jnp.arange(local_rows, dtype=jnp.int32))
    mirror_out = jnp.swapaxes(held[inverse], 1, 2)
    chunk = local_rows // cols
    span = chunk * bs
    tags = jnp.zeros((cols, EXTRA, bs), jnp.float32).at[:, 0, :chunk].set(
        own_cols.astype(jnp.float32).reshape(cols, chunk)
    )
    pieces = jnp.concatenate([
        held.reshape(cols, span, bs),
        mirror_out.reshape(cols, span, bs),
        tags,
    ], axis=1)
    spread = lax.all_to_all(pieces, "col", 0, 0, tiled=True)
    first = jnp.swapaxes(spread[:, :span].reshape(cols, chunk, bs, bs), 0, 1)
    second = lax.all_to_all(first, "row", 1, 1, tiled=True)
    arrived = lax.all_to_all(second, "col", 1, 0, tiled=True).reshape(local_rows, bs, bs)
    density = held + jnp.swapaxes(arrived[own_cols], 1, 2)
    mine = []
    for step in range(STEPS):
        own = lax.dynamic_index_in_dim(spread, (row_index + step) % cols, 0, keepdims=False)
        far = lax.dynamic_index_in_dim(spread, (row_index - step) % cols, 0, keepdims=False)[span:2 * span]
        if step:
            far = shifted(far, "row", step)
        blocks = (own[:span] + far).reshape(chunk, bs, bs)
        marks = jnp.zeros((chunk, EXTRA, bs), jnp.float32).at[:, 0, 0].set(own[2 * span, :chunk])
        mine.append(jnp.concatenate([blocks, marks], axis=1))
    mine = jnp.stack(mine)
    left_all = lax.all_gather(mine, "col", axis=0, tiled=False)
    left_all = jnp.transpose(left_all, (1, 0, 2, 3, 4)).reshape(STEPS, local_rows, bs + EXTRA, bs)

    one = shifted(density, "row", 1)
    two = shifted(density, "row", 2)
    three = shifted(two, "row", 1)
    rights = [density, one, two, three]
    cols_two = shifted(own_cols, "row", 2)
    right_cols = [own_cols, shifted(own_cols, "row", 1), cols_two, shifted(cols_two, "row", 1)]

    total = jnp.zeros((local_rows, bs, bs), jnp.float32)
    for step in range(STEPS):
        left = left_all[step]
        inner = left[:, bs, 0].astype(jnp.int32)
        right = rights[step][inner]
        match = right_cols[step][inner] == own_cols
        masked = jnp.where(match[:, None, None], left[:, :bs], jnp.float32(0.0))
        total = total + jnp.einsum("rik,rkj->rij", masked, right, precision=lax.Precision.HIGH)
    return total[:, None]


def solution(mesh):
    return jax.shard_map(
        shards,
        mesh=mesh,
        in_specs=(P("row", "col", None, None), P("row", "col"), P("row", "col")),
        out_specs=P("row", "col", None, None),
        check_vma=False,
    )
```
